256 devices in a mesh: sub: 64 (over z, x, core), row: 4 (over y).
Axes of the slice: x: 4, y: 4, z: 8, core: 2. Of those that a mesh axis runs over, the one named last changes fastest.
Arguments:
- residual: float32 [32, 64, 2048], P(None, 'sub', 'row')
- factor: float32 [64, 3072, 3072], P('sub', 'row'), may hold values from -0.0390625 to 0.0390625
- basis: float32 [96, 64, 2048], P(None, 'sub', 'row'), may hold values from -0.015625 to 0.015625
- send_rows: int32 [64, 2, 512], P('sub'), may hold values from 0 to 2047, as said below
Outputs:
- coeffs: float32 [96, 32], replicated
- rfactor: float32 [32, 32], replicated
- block_q: float32 [32, 64, 2048], P(None, 'sub', 'row')
The draws below stay inside these ranges and needn't reach their ends.
Inputs may be any that keep to these rules, and one draw needn't show every extreme that they name: Within each send_rows[s, side, :] the rows are distinct.
All inputs are finite; a program needn't handle non-finite values.
Results may differ from the reference program's by a relative error of at most 0.000073.
Values sent between devices are 32-bit elements; how exact they have to be, the bound alone decides.
No kernel may reach another device: no remote copies, remote signals or barrier semaphores. Data moves between devices by JAX's collectives and lax.ppermute only.
A program may use at most 64 MiB of HBM per device.

```python
import math
import jax
import jax.numpy as jnp
from jax import lax

VECS = 32
BASIS = 96
OV = 512
SUBS = 64
SUB_ROWS = 2048
EXT = 3072
ROWS = 131072


def draw_residual(key, part):
    key_noise, key_cell = jax.random.split(key, 2)
    position = jnp.arange(SUBS, dtype=jnp.float32) / (SUBS - 1)
    trend = (1.0 + 2.0 * position)[None, :, None]
    cell = jnp.exp(math.log(10.0) * jax.random.uniform(key_cell, (1, SUBS, SUB_ROWS), jnp.float32))
    noise = jax.random.normal(key_noise, (VECS, SUBS, SUB_ROWS), jnp.float32)
    values = noise * cell * trend * 0.1
    return values.astype(jnp.float32)


def draw_send_rows(key, part):
    keys = jax.random.split(jax.random.fold_in(key, 7), SUBS * 2)
    picked = jax.vmap(lambda one_key: jax.random.permutation(one_key, SUB_ROWS)[:OV])(keys)
    return picked.reshape(SUBS, 2, OV).astype(jnp.int32)


def steps_of(key, extent, shards, smallest, top_value):
    gain = 1.0
    for dim, parts in shards:
        draws = jax.random.uniform(jax.random.fold_in(jax.random.fold_in(key, 6), dim), (parts,), jnp.float32, smallest / len(shards), top_value / len(shards))
        gain = gain * jnp.repeat(jnp.exp(draws), extent[dim] // parts).reshape((-1,) + (1,) * (len(extent) - 1 - dim))
    return gain


def normal_values(key, extent, deviation, limit, pieces=(), kind=jnp.bfloat16):
    drawn = deviation * jax.random.normal(key, extent, jnp.float32)
    if pieces:
        drawn = drawn * steps_of(key, extent, pieces, -0.22, 0.18)
    return jnp.clip(drawn, -limit, limit).astype(kind)


def setup_inputs(seed: int = 0) -> dict:
    key_of = jax.random.split(jax.random.key(seed), 5)
    residual = draw_residual(jax.random.fold_in(key_of[4], 71), 0)
    factor = normal_values(key_of[1], (SUBS, EXT, EXT), (8 * EXT) ** -0.5, 0.0390625, ((0, 64), (1, 4)), jnp.float32)
    basis = normal_values(key_of[2], (BASIS, SUBS, SUB_ROWS), ROWS ** -0.5, 0.015625, ((1, 64), (2, 4)), jnp.float32)
    send_rows = draw_send_rows(jax.random.fold_in(key_of[4], 71), 0)
    return {"residual": residual, "factor": factor, "basis": basis, "send_rows": send_rows}


HIGH = lax.Precision.HIGHEST

def apply_block(pair):
    extended, factor_block = pair
    size = factor_block.shape[0]
    full = factor_block + jnp.eye(size, dtype=factor_block.dtype)
    inner = lax.dot_general(extended, full, (((1,), (1,)), ((), ())), precision=HIGH)
    return jnp.dot(inner, full, precision=HIGH)

def pick_rows(block, rows_index):
    return block[:, rows_index]

def add_rows(block, values, rows_index):
    return block.at[:, rows_index].add(values)

def reference(residual, factor, basis, send_rows):
    zero_rim = jnp.zeros((VECS, 1, OV), residual.dtype)
    to_lower = jax.vmap(pick_rows, in_axes=(1, 0), out_axes=1)(residual, send_rows[:, 0])
    to_upper = jax.vmap(pick_rows, in_axes=(1, 0), out_axes=1)(residual, send_rows[:, 1])
    from_lower = jnp.concatenate([zero_rim, to_upper[:, :-1]], axis=1)
    from_upper = jnp.concatenate([to_lower[:, 1:], zero_rim], axis=1)
    extended = jnp.concatenate([residual, from_lower, from_upper], axis=2)
    local = lax.map(apply_block, (jnp.transpose(extended, (1, 0, 2)), factor))
    own_part = local[:, :, :SUB_ROWS]
    lower_part = local[:, :, SUB_ROWS:SUB_ROWS + OV]
    upper_part = local[:, :, SUB_ROWS + OV:]
    zero_back = jnp.zeros((1, VECS, OV), residual.dtype)
    back_from_upper = jnp.concatenate([lower_part[1:], zero_back], axis=0)
    back_from_lower = jnp.concatenate([zero_back, upper_part[:-1]], axis=0)
    summed = jax.vmap(add_rows)(own_part, back_from_upper, send_rows[:, 1])
    summed = jax.vmap(add_rows)(summed, back_from_lower, send_rows[:, 0])
    block_t = jnp.transpose(summed, (1, 0, 2)).reshape(VECS, ROWS)
    vectors = basis.reshape(BASIS, ROWS)
    first = lax.dot_general(vectors, block_t, (((1,), (1,)), ((), ())), precision=HIGH)
    once = block_t - lax.dot_general(first, vectors, (((0,), (0,)), ((), ())), precision=HIGH)
    second = lax.dot_general(vectors, once, (((1,), (1,)), ((), ())), precision=HIGH)
    twice = once - lax.dot_general(second, vectors, (((0,), (0,)), ((), ())), precision=HIGH)
    gram = lax.dot_general(twice, twice, (((1,), (1,)), ((), ())), precision=HIGH) / ROWS
    lower_tri = jnp.linalg.cholesky(gram)
    solved = jax.scipy.linalg.solve_triangular(lower_tri, twice, lower=True)
    return (first + second, lower_tri.T, solved.reshape(VECS, SUBS, SUB_ROWS))
```

```python
import jax
import jax.numpy as jnp
from jax import lax
from jax.sharding import PartitionSpec as P

HIGH = lax.Precision.HIGHEST


def from_behind(value, axis, steps):
    count = lax.axis_size(axis)
    leading, last = (max(0, -steps), min(count, count - steps))
    return lax.ppermute(value, axis, [(source, source + steps) for source in range(leading, last)])


def swap(value, axis, mask):
    count = lax.axis_size(axis)
    return lax.ppermute(value, axis, [(source, source ^ mask) for source in range(count)])


def contract_rows(left_mat, right_mat):
    return lax.dot_general(left_mat, right_mat, (((1,), (1,)), ((), ())), precision=HIGH)


def contract_first(left_mat, right_mat):
    return lax.dot_general(left_mat, right_mat, (((0,), (0,)), ((), ())), precision=HIGH)


def gather_rows(own, axis):
    pos = lax.axis_index(axis)
    block = own
    step = 1
    while step < lax.axis_size(axis):
        other = swap(block, axis, step)
        upper = (pos & step) != 0
        block = jnp.where(upper, jnp.concatenate([other, block], axis=1), jnp.concatenate([block, other], axis=1))
        step *= 2
    return block


def scatter_rows(value, axis):
    pos = lax.axis_index(axis)
    step = lax.axis_size(axis) // 2
    block = value
    while step >= 1:
        half = block.shape[1] // 2
        upper = ((pos // step) % 2).astype(jnp.int32)
        keep = lax.dynamic_slice_in_dim(block, upper * half, half, 1)
        send = lax.dynamic_slice_in_dim(block, (1 - upper) * half, half, 1)
        block = keep + swap(send, axis, step)
        step //= 2
    return block


def all_sum(value, axes):
    for axis in axes:
        step = 1
        while step < lax.axis_size(axis):
            value = value + swap(value, axis, step)
            step *= 2
    return value


def per_device(residual, factor, basis, send_rows):
    slab = residual.shape[2]
    row_count = lax.axis_size("row")
    sub_rows = slab * row_count
    total_rows = sub_rows * lax.axis_size("sub")
    own_rows = residual[:, 0, :]
    whole = gather_rows(own_rows, "row")
    index_rows = send_rows[0]
    to_lower = jnp.take(whole, index_rows[0], axis=1)
    to_upper = jnp.take(whole, index_rows[1], axis=1)
    from_lower = from_behind(to_upper, "sub", 1)
    from_upper = from_behind(to_lower, "sub", -1)
    extended = jnp.concatenate([whole, from_lower, from_upper], axis=1)
    factor_rows = factor[0]
    share = factor_rows.shape[0]
    margin = from_lower.shape[1]
    row_pos = lax.axis_index("row")
    global_rows = row_pos * share + lax.iota(jnp.int32, share)
    columns = lax.iota(jnp.int32, factor_rows.shape[1])
    full = factor_rows + (global_rows[:, None] == columns[None, :]).astype(jnp.float32)
    inner = contract_rows(extended, full)
    partial_value = jnp.dot(inner, full, precision=HIGH)
    back_upper = from_behind(partial_value[:, sub_rows:sub_rows + margin], "sub", -1)
    back_lower = from_behind(partial_value[:, sub_rows + margin:], "sub", 1)
    all_rows = lax.iota(jnp.int32, sub_rows)
    select_upper = (index_rows[1][:, None] == all_rows[None, :]).astype(jnp.float32)
    select_lower = (index_rows[0][:, None] == all_rows[None, :]).astype(jnp.float32)
    gathered = (
        partial_value[:, :sub_rows]
        + jnp.dot(back_upper, select_upper, precision=HIGH)
        + jnp.dot(back_lower, select_lower, precision=HIGH)
    )
    block_t = scatter_rows(gathered, "row")
    vectors = basis[:, 0, :]
    count = vectors.shape[0]
    vecs = block_t.shape[0]
    first_part = contract_rows(vectors, block_t)
    basis_gram = contract_rows(vectors, vectors)
    block_gram = contract_rows(block_t, block_t)
    packed = jnp.concatenate(
        [
            jnp.concatenate([first_part, basis_gram], axis=1),
            jnp.concatenate([block_gram, jnp.zeros((vecs, count), jnp.float32)], axis=1),
        ],
        axis=0,
    )
    summed = all_sum(packed, ("sub", "row"))
    first, basis_gram, block_gram = lax.optimization_barrier(
        (summed[:count, :vecs], summed[:count, vecs:], summed[count:, :vecs])
    )
    second = first - jnp.dot(basis_gram, first, precision=HIGH)
    coeffs = first + second
    once = block_t - contract_first(first, vectors)
    twice = once - contract_first(second, vectors)
    cross = contract_first(first, coeffs)
    gram = (
        block_gram - cross - cross.T + contract_first(coeffs, jnp.dot(basis_gram, coeffs, precision=HIGH))
    ) / total_rows
    lower_tri = jnp.linalg.cholesky(gram)
    solved = jax.scipy.linalg.solve_triangular(lower_tri, twice, lower=True)
    return (coeffs, lower_tri.T, solved[:, None, :])


def solution(mesh):
    placed = (
        P(None, "sub", "row"),
        P("sub", "row", None),
        P(None, "sub", "row"),
        P("sub", None, None),
    )
    return jax.shard_map(
        per_device,
        mesh=mesh,
        in_specs=placed,
        out_specs=(P(), P(), P(None, "sub", "row")),
        check_vma=False,
    )
```

```python
import jax
import jax.numpy as jnp
from jax import lax
from jax.sharding import PartitionSpec as P

HIGH = lax.Precision.HIGHEST


def from_behind(value, axis, steps):
    count = lax.axis_size(axis)
    leading, last = (max(0, -steps), min(count, count - steps))
    return lax.ppermute(value, axis, [(source, source + steps) for source in range(leading, last)])


def swap(value, axis, mask):
    count = lax.axis_size(axis)
    return lax.ppermute(value, axis, [(source, source ^ mask) for source in range(count)])


def contract_rows(left_mat, right_mat):
    return lax.dot_general(left_mat, right_mat, (((1,), (1,)), ((), ())), precision=HIGH)


def contract_first(left_mat, right_mat):
    return lax.dot_general(left_mat, right_mat, (((0,), (0,)), ((), ())), precision=HIGH)


def gather_rows(own, axis):
    pos = lax.axis_index(axis)
    block = own
    step = 1
    while step < lax.axis_size(axis):
        other = swap(block, axis, step)
        upper = (pos & step) != 0
        block = jnp.where(upper, jnp.concatenate([other, block], axis=1), jnp.concatenate([block, other], axis=1))
        step *= 2
    return block


def scatter_rows(value, axis):
    pos = lax.axis_index(axis)
    step = lax.axis_size(axis) // 2
    block = value
    while step >= 1:
        half = block.shape[1] // 2
        upper = ((pos // step) % 2).astype(jnp.int32)
        keep = lax.dynamic_slice_in_dim(block, upper * half, half, 1)
        send = lax.dynamic_slice_in_dim(block, (1 - upper) * half, half, 1)
        block = keep + swap(send, axis, step)
        step //= 2
    return block


def all_sum(value, axes):
    for axis in axes:
        step = 1
        while step < lax.axis_size(axis):
            value = value + swap(value, axis, step)
            step *= 2
    return value


def per_device(residual, factor, basis, send_rows):
    slab = residual.shape[2]
    row_count = lax.axis_size("row")
    sub_rows = slab * row_count
    total_rows = sub_rows * lax.axis_size("sub")
    own_rows = residual[:, 0, :]
    whole = gather_rows(own_rows, "row")
    index_rows = send_rows[0]
    to_lower = jnp.take(whole, index_rows[0], axis=1)
    to_upper = jnp.take(whole, index_rows[1], axis=1)
    from_lower = from_behind(to_upper, "sub", 1)
    from_upper = from_behind(to_lower, "sub", -1)
    extended = jnp.concatenate([whole, from_lower, from_upper], axis=1)
    factor_rows = factor[0]
    share = factor_rows.shape[0]
    margin = from_lower.shape[1]
    row_pos = lax.axis_index("row")
    start = row_pos * share
    inner = lax.dynamic_slice_in_dim(extended, start, share, 1) + lax.dot_general(
        extended, factor_rows, (((1,), (1,)), ((), ())), precision=lax.Precision.HIGH
    )
    product = jnp.dot(inner, factor_rows, precision=lax.Precision.HIGH)
    partial_value = lax.dynamic_update_slice_in_dim(
        product, lax.dynamic_slice_in_dim(product, start, share, 1) + inner, start, 1
    )
    back_upper = from_behind(partial_value[:, sub_rows:sub_rows + margin], "sub", -1)
    back_lower = from_behind(partial_value[:, sub_rows + margin:], "sub", 1)
    all_rows = lax.iota(jnp.int32, sub_rows)
    select_upper = (index_rows[1][:, None] == all_rows[None, :]).astype(jnp.float32)
    select_lower = (index_rows[0][:, None] == all_rows[None, :]).astype(jnp.float32)
    gathered = (
        partial_value[:, :sub_rows]
        + jnp.dot(back_upper, select_upper, precision=HIGH)
        + jnp.dot(back_lower, select_lower, precision=HIGH)
    )
    block_t = scatter_rows(gathered, "row")
    vectors = basis[:, 0, :]
    count = vectors.shape[0]
    vecs = block_t.shape[0]
    first_part = contract_rows(vectors, block_t)
    basis_gram = contract_rows(vectors, vectors)
    block_gram = contract_rows(block_t, block_t)
    packed = jnp.concatenate(
        [
            jnp.concatenate([first_part, basis_gram], axis=1),
            jnp.concatenate([block_gram, jnp.zeros((vecs, count), jnp.float32)], axis=1),
        ],
        axis=0,
    )
    summed = all_sum(packed, ("sub", "row"))
    first, basis_gram, block_gram = lax.optimization_barrier(
        (summed[:count, :vecs], summed[:count, vecs:], summed[count:, :vecs])
    )
    second = first - jnp.dot(basis_gram, first, precision=HIGH)
    coeffs = first + second
    once = block_t - contract_first(first, vectors)
    twice = once - contract_first(second, vectors)
    cross = contract_first(first, coeffs)
    gram = (
        block_gram - cross - cross.T + contract_first(coeffs, jnp.dot(basis_gram, coeffs, precision=HIGH))
    ) / total_rows
    lower_tri = jnp.linalg.cholesky(gram)
    solved = jax.scipy.linalg.solve_triangular(lower_tri, twice, lower=True)
    return (coeffs, lower_tri.T, solved[:, None, :])


def solution(mesh):
    placed = (
        P(None, "sub", "row"),
        P("sub", "row", None),
        P(None, "sub", "row"),
        P("sub", None, None),
    )
    return jax.shard_map(
        per_device,
        mesh=mesh,
        in_specs=placed,
        out_specs=(P(), P(), P(None, "sub", "row")),
        check_vma=False,
    )
```

```python
import jax
import jax.numpy as jnp
from jax import lax
from jax.sharding import PartitionSpec as P

HIGH = lax.Precision.HIGHEST


def from_behind(value, axis, steps):
    count = lax.axis_size(axis)
    leading, last = (max(0, -steps), min(count, count - steps))
    return lax.ppermute(value, axis, [(source, source + steps) for source in range(leading, last)])


def swap(value, axis, mask):
    count = lax.axis_size(axis)
    return lax.ppermute(value, axis, [(source, source ^ mask) for source in range(count)])


def contract_rows(left_mat, right_mat):
    return lax.dot_general(left_mat, right_mat, (((1,), (1,)), ((), ())), precision=HIGH)


def contract_first(left_mat, right_mat):
    return lax.dot_general(left_mat, right_mat, (((0,), (0,)), ((), ())), precision=HIGH)


def ring_masks(size):
    near = {2: [1], 4: [1, 3], 8: [1, 2, 6]}
    masks = near.get(size) or [1 << b for b in range(size.bit_length() - 1)]
    return [(1 << b, mask) for b, mask in enumerate(masks)]


def gather_rows(own, axis):
    pos = lax.axis_index(axis)
    block = own
    for step, mask in ring_masks(lax.axis_size(axis)):
        other = swap(block, axis, mask)
        upper = (pos & step) != 0
        block = jnp.where(upper, jnp.concatenate([other, block], axis=1), jnp.concatenate([block, other], axis=1))
    return block


def scatter_rows(value, axis):
    pos = lax.axis_index(axis)
    block = value
    for step, mask in reversed(ring_masks(lax.axis_size(axis))):
        half = block.shape[1] // 2
        upper = ((pos // step) % 2).astype(jnp.int32)
        keep = lax.dynamic_slice_in_dim(block, upper * half, half, 1)
        send = lax.dynamic_slice_in_dim(block, (1 - upper) * half, half, 1)
        block = keep + swap(send, axis, mask)
    return block


def all_sum(value, axes):
    for axis, rings in axes:
        masks = [0]
        scale = 1
        for ring in rings:
            masks += [mask * scale for _, mask in ring_masks(ring)]
            scale *= ring
        for mask in masks[1:]:
            value = value + swap(value, axis, mask)
    return value


def per_device(residual, factor, basis, send_rows):
    slab = residual.shape[2]
    row_count = lax.axis_size("row")
    sub_rows = slab * row_count
    total_rows = sub_rows * lax.axis_size("sub")
    own_rows = residual[:, 0, :]
    whole = gather_rows(own_rows, "row")
    index_rows = send_rows[0]
    to_lower = jnp.take(whole, index_rows[0], axis=1)
    to_upper = jnp.take(whole, index_rows[1], axis=1)
    from_lower = from_behind(to_upper, "sub", 1)
    from_upper = from_behind(to_lower, "sub", -1)
    extended = jnp.concatenate([whole, from_lower, from_upper], axis=1)
    factor_rows = factor[0]
    share = factor_rows.shape[0]
    margin = from_lower.shape[1]
    row_pos = lax.axis_index("row")
    start = row_pos * share
    inner = lax.dynamic_slice_in_dim(extended, start, share, 1) + lax.dot_general(
        extended, factor_rows, (((1,), (1,)), ((), ())), precision=lax.Precision.HIGH
    )
    product = jnp.dot(inner, factor_rows, precision=lax.Precision.HIGH)
    partial_value = lax.dynamic_update_slice_in_dim(
        product, lax.dynamic_slice_in_dim(product, start, share, 1) + inner, start, 1
    )
    back_upper = from_behind(partial_value[:, sub_rows:sub_rows + margin], "sub", -1)
    back_lower = from_behind(partial_value[:, sub_rows + margin:], "sub", 1)
    all_rows = lax.iota(jnp.int32, sub_rows)
    select_upper = (index_rows[1][:, None] == all_rows[None, :]).astype(jnp.float32)
    select_lower = (index_rows[0][:, None] == all_rows[None, :]).astype(jnp.float32)
    gathered = (
        partial_value[:, :sub_rows]
        + jnp.dot(back_upper, select_upper, precision=HIGH)
        + jnp.dot(back_lower, select_lower, precision=HIGH)
    )
    block_t = scatter_rows(gathered, "row")
    vectors = basis[:, 0, :]
    count = vectors.shape[0]
    vecs = block_t.shape[0]
    first_part = contract_rows(vectors, block_t)
    basis_gram = contract_rows(vectors, vectors)
    block_gram = contract_rows(block_t, block_t)
    packed = jnp.concatenate(
        [
            jnp.concatenate([first_part, basis_gram], axis=1),
            jnp.concatenate([block_gram, jnp.zeros((vecs, count), jnp.float32)], axis=1),
        ],
        axis=0,
    )
    summed = all_sum(packed, (("sub", (2, 4, lax.axis_size("sub") // 8)), ("row", (row_count,))))
    first, basis_gram, block_gram = lax.optimization_barrier(
        (summed[:count, :vecs], summed[:count, vecs:], summed[count:, :vecs])
    )
    second = first - jnp.dot(basis_gram, first, precision=HIGH)
    coeffs = first + second
    once = block_t - contract_first(first, vectors)
    twice = once - contract_first(second, vectors)
    cross = contract_first(first, coeffs)
    gram = (
        block_gram - cross - cross.T + contract_first(coeffs, jnp.dot(basis_gram, coeffs, precision=HIGH))
    ) / total_rows
    lower_tri = jnp.linalg.cholesky(gram)
    solved = jax.scipy.linalg.solve_triangular(lower_tri, twice, lower=True)
    return (coeffs, lower_tri.T, solved[:, None, :])


def solution(mesh):
    placed = (
        P(None, "sub", "row"),
        P("sub", "row", None),
        P(None, "sub", "row"),
        P("sub", None, None),
    )
    return jax.shard_map(
        per_device,
        mesh=mesh,
        in_specs=placed,
        out_specs=(P(), P(), P(None, "sub", "row")),
        check_vma=False,
    )
```

```python
import jax
import jax.numpy as jnp
from jax import lax
from jax.sharding import PartitionSpec as P

HIGH = lax.Precision.HIGHEST


def from_behind(value, axis, steps):
    count = lax.axis_size(axis)
    leading, last = (max(0, -steps), min(count, count - steps))
    return lax.ppermute(value, axis, [(source, source + steps) for source in range(leading, last)])


def swap(value, axis, mask):
    count = lax.axis_size(axis)
    return lax.ppermute(value, axis, [(source, source ^ mask) for source in range(count)])


def contract_rows(left_mat, right_mat):
    return lax.dot_general(left_mat, right_mat, (((1,), (1,)), ((), ())), precision=HIGH)


def contract_first(left_mat, right_mat):
    return lax.dot_general(left_mat, right_mat, (((0,), (0,)), ((), ())), precision=HIGH)


def ring_masks(size):
    near = {2: [1], 4: [1, 3], 8: [1, 2, 6]}
    masks = near.get(size) or [1 << b for b in range(size.bit_length() - 1)]
    return [(1 << b, mask) for b, mask in enumerate(masks)]


def gather_rows(own, axis):
    pos = lax.axis_index(axis)
    block = own
    for step, mask in ring_masks(lax.axis_size(axis)):
        other = swap(block, axis, mask)
        upper = (pos & step) != 0
        block = jnp.where(upper, jnp.concatenate([other, block], axis=1), jnp.concatenate([block, other], axis=1))
    return block


def scatter_rows(value, axis):
    pos = lax.axis_index(axis)
    block = value
    for step, mask in reversed(ring_masks(lax.axis_size(axis))):
        half = block.shape[1] // 2
        upper = ((pos // step) % 2).astype(jnp.int32)
        keep = lax.dynamic_slice_in_dim(block, upper * half, half, 1)
        send = lax.dynamic_slice_in_dim(block, (1 - upper) * half, half, 1)
        block = keep + swap(send, axis, mask)
    return block


def all_sum(value, axes):
    for axis, rings in axes:
        masks = [0]
        scale = 1
        for ring in rings:
            masks += [mask * scale for _, mask in ring_masks(ring)]
            scale *= ring
        for mask in masks[1:]:
            value = value + swap(value, axis, mask)
    return value


def per_device(residual, factor, basis, send_rows):
    slab = residual.shape[2]
    row_count = lax.axis_size("row")
    sub_rows = slab * row_count
    total_rows = sub_rows * lax.axis_size("sub")
    own_rows = residual[:, 0, :]
    whole = gather_rows(own_rows, "row")
    index_rows = send_rows[0]
    to_lower = jnp.take(whole, index_rows[0], axis=1)
    to_upper = jnp.take(whole, index_rows[1], axis=1)
    from_lower = from_behind(to_upper, "sub", 1)
    from_upper = from_behind(to_lower, "sub", -1)
    extended = jnp.concatenate([whole, from_lower, from_upper], axis=1)
    factor_rows = factor[0]
    share = factor_rows.shape[0]
    margin = from_lower.shape[1]
    row_pos = lax.axis_index("row")
    start = row_pos * share
    inner = lax.dynamic_slice_in_dim(extended, start, share, 1) + lax.dot_general(
        extended, factor_rows, (((1,), (1,)), ((), ())), precision=lax.Precision.HIGH
    )
    product = jnp.dot(inner, factor_rows, precision=lax.Precision.HIGH)
    partial_value = lax.dynamic_update_slice_in_dim(
        product, lax.dynamic_slice_in_dim(product, start, share, 1) + inner, start, 1
    )
    back_upper = from_behind(partial_value[:, sub_rows:sub_rows + margin], "sub", -1)
    back_lower = from_behind(partial_value[:, sub_rows + margin:], "sub", 1)
    all_rows = lax.iota(jnp.int32, sub_rows)
    select_upper = (index_rows[1][:, None] == all_rows[None, :]).astype(jnp.float32)
    select_lower = (index_rows[0][:, None] == all_rows[None, :]).astype(jnp.float32)
    gathered = partial_value[:, :sub_rows] + jnp.dot(
        jnp.concatenate([back_upper, back_lower], axis=1),
        jnp.concatenate([select_upper, select_lower], axis=0),
        precision=HIGH,
    )
    block_t = scatter_rows(gathered, "row")
    vectors = basis[:, 0, :]
    count = vectors.shape[0]
    vecs = block_t.shape[0]
    first_part = contract_rows(vectors, block_t)
    basis_gram = contract_rows(vectors, vectors)
    block_gram = contract_rows(block_t, block_t)
    corner = count - vecs
    packed = jnp.concatenate([first_part, basis_gram.at[corner:, :vecs].set(block_gram)], axis=1)
    summed = all_sum(packed, (("sub", (2, 4, lax.axis_size("sub") // 8)), ("row", (row_count,))))
    first, basis_gram, block_gram = lax.optimization_barrier(
        (summed[:, :vecs], summed[:, vecs:], summed[corner:, vecs:vecs + vecs])
    )
    basis_gram = basis_gram.at[corner:, :vecs].set(basis_gram[:vecs, corner:].T)
    second = first - jnp.dot(basis_gram, first, precision=HIGH)
    coeffs = first + second
    once = block_t - contract_first(first, vectors)
    twice = once - contract_first(second, vectors)
    cross = contract_first(first, coeffs)
    gram = (
        block_gram - cross - cross.T + contract_first(coeffs, jnp.dot(basis_gram, coeffs, precision=HIGH))
    ) / total_rows
    lower_tri = jnp.linalg.cholesky(gram)
    solved = jax.scipy.linalg.solve_triangular(lower_tri, twice, lower=True)
    return (coeffs, lower_tri.T, solved[:, None, :])


def solution(mesh):
    placed = (
        P(None, "sub", "row"),
        P("sub", "row", None),
        P(None, "sub", "row"),
        P("sub", None, None),
    )
    return jax.shard_map(
        per_device,
        mesh=mesh,
        in_specs=placed,
        out_specs=(P(), P(), P(None, "sub", "row")),
        check_vma=False,
    )
```

```python
import jax
import jax.numpy as jnp
from jax import lax
from jax.sharding import PartitionSpec as P

HIGH = lax.Precision.HIGHEST


def from_behind(value, axis, steps):
    count = lax.axis_size(axis)
    leading, last = (max(0, -steps), min(count, count - steps))
    return lax.ppermute(value, axis, [(source, source + steps) for source in range(leading, last)])


def swap(value, axis, mask):
    count = lax.axis_size(axis)
    return lax.ppermute(value, axis, [(source, source ^ mask) for source in range(count)])


def contract_rows(left_mat, right_mat):
    return lax.dot_general(left_mat, right_mat, (((1,), (1,)), ((), ())), precision=HIGH)


def contract_first(left_mat, right_mat):
    return lax.dot_general(left_mat, right_mat, (((0,), (0,)), ((), ())), precision=HIGH)


def ring_masks(size):
    near = {2: [1], 4: [1, 3], 8: [1, 2, 6]}
    masks = near.get(size) or [1 << b for b in range(size.bit_length() - 1)]
    return [(1 << b, mask) for b, mask in enumerate(masks)]


def gather_rows(own, axis):
    pos = lax.axis_index(axis)
    block = own
    for step, mask in ring_masks(lax.axis_size(axis)):
        other = swap(block, axis, mask)
        upper = (pos & step) != 0
        block = jnp.where(upper, jnp.concatenate([other, block], axis=1), jnp.concatenate([block, other], axis=1))
    return block


def scatter_rows(value, axis):
    pos = lax.axis_index(axis)
    block = value
    for step, mask in reversed(ring_masks(lax.axis_size(axis))):
        half = block.shape[1] // 2
        upper = ((pos // step) % 2).astype(jnp.int32)
        keep = lax.dynamic_slice_in_dim(block, upper * half, half, 1)
        send = lax.dynamic_slice_in_dim(block, (1 - upper) * half, half, 1)
        block = keep + swap(send, axis, mask)
    return block


def all_sum(value, axes):
    for axis, rings in axes:
        masks = [0]
        scale = 1
        for ring in rings:
            masks += [mask * scale for _, mask in ring_masks(ring)]
            scale *= ring
        for mask in masks[1:]:
            value = value + swap(value, axis, mask)
    return value


def per_device(residual, factor, basis, send_rows):
    slab = residual.shape[2]
    row_count = lax.axis_size("row")
    sub_rows = slab * row_count
    total_rows = sub_rows * lax.axis_size("sub")
    own_rows = residual[:, 0, :]
    whole = gather_rows(own_rows, "row")
    index_rows = send_rows[0]
    to_lower = jnp.take(whole, index_rows[0], axis=1)
    to_upper = jnp.take(whole, index_rows[1], axis=1)
    from_lower = from_behind(to_upper, "sub", 1)
    from_upper = from_behind(to_lower, "sub", -1)
    factor_rows = factor[0]
    share = factor_rows.shape[0]
    margin = from_lower.shape[1]
    row_pos = lax.axis_index("row")
    three = lax.Precision.HIGH
    by_rows = (((1,), (1,)), ((), ()))
    start = row_pos * share
    inner_own = lax.optimization_barrier(lax.dot_general(whole, factor_rows[:, :sub_rows], by_rows, precision=three))
    margins = jnp.concatenate([from_lower, from_upper], axis=1)
    extended = jnp.concatenate([whole, margins], axis=1)
    inner = (
        inner_own
        + lax.dot_general(margins, factor_rows[:, sub_rows:], by_rows, precision=three)
        + lax.dynamic_slice_in_dim(extended, start, share, 1)
    )
    placed = lax.dynamic_update_slice_in_dim(jnp.zeros(extended.shape, jnp.float32), inner, start, 1)
    margin_value = jnp.dot(inner, factor_rows[:, sub_rows:], precision=three) + placed[:, sub_rows:]
    back_upper = from_behind(margin_value[:, :margin], "sub", -1)
    back_lower = from_behind(margin_value[:, margin:], "sub", 1)
    own_value = jnp.dot(inner, factor_rows[:, :sub_rows], precision=three) + placed[:, :sub_rows]
    all_rows = lax.iota(jnp.int32, sub_rows)
    select_upper = (index_rows[1][:, None] == all_rows[None, :]).astype(jnp.float32)
    select_lower = (index_rows[0][:, None] == all_rows[None, :]).astype(jnp.float32)
    gathered = (
        own_value
        + jnp.dot(back_upper, select_upper, precision=HIGH)
        + jnp.dot(back_lower, select_lower, precision=HIGH)
    )
    block_t = scatter_rows(gathered, "row")
    vectors = basis[:, 0, :]
    count = vectors.shape[0]
    vecs = block_t.shape[0]
    first_part = contract_rows(vectors, block_t)
    basis_gram = contract_rows(vectors, vectors)
    block_gram = contract_rows(block_t, block_t)
    packed = jnp.concatenate(
        [
            jnp.concatenate([first_part, basis_gram], axis=1),
            jnp.concatenate([block_gram, jnp.zeros((vecs, count), jnp.float32)], axis=1),
        ],
        axis=0,
    )
    summed = all_sum(packed, (("sub", (2, 4, lax.axis_size("sub") // 8)), ("row", (row_count,))))
    first, basis_gram, block_gram = lax.optimization_barrier(
        (summed[:count, :vecs], summed[:count, vecs:], summed[count:, :vecs])
    )
    second = first - jnp.dot(basis_gram, first, precision=HIGH)
    coeffs = first + second
    once = block_t - contract_first(first, vectors)
    twice = once - contract_first(second, vectors)
    cross = contract_first(first, coeffs)
    gram = (
        block_gram - cross - cross.T + contract_first(coeffs, jnp.dot(basis_gram, coeffs, precision=HIGH))
    ) / total_rows
    lower_tri = jnp.linalg.cholesky(gram)
    solved = jax.scipy.linalg.solve_triangular(lower_tri, twice, lower=True)
    return (coeffs, lower_tri.T, solved[:, None, :])


def solution(mesh):
    placed = (
        P(None, "sub", "row"),
        P("sub", "row", None),
        P(None, "sub", "row"),
        P("sub", None, None),
    )
    return jax.shard_map(
        per_device,
        mesh=mesh,
        in_specs=placed,
        out_specs=(P(), P(), P(None, "sub", "row")),
        check_vma=False,
    )
```

```python
import jax
import jax.numpy as jnp
from jax import lax
from jax.experimental import pallas as pl
from jax.sharding import PartitionSpec as P

HIGH = lax.Precision.HIGHEST


def from_behind(value, axis, steps):
    count = lax.axis_size(axis)
    leading, last = (max(0, -steps), min(count, count - steps))
    return lax.ppermute(value, axis, [(source, source + steps) for source in range(leading, last)])


def swap(value, axis, mask):
    count = lax.axis_size(axis)
    return lax.ppermute(value, axis, [(source, source ^ mask) for source in range(count)])


def contract_rows(left_mat, right_mat):
    return lax.dot_general(left_mat, right_mat, (((1,), (1,)), ((), ())), precision=HIGH)


def contract_first(left_mat, right_mat):
    return lax.dot_general(left_mat, right_mat, (((0,), (0,)), ((), ())), precision=HIGH)


def ring_masks(size):
    near = {2: [1], 4: [1, 3], 8: [1, 2, 6]}
    masks = near.get(size) or [1 << b for b in range(size.bit_length() - 1)]
    return [(1 << b, mask) for b, mask in enumerate(masks)]


def gather_rows(own, axis):
    pos = lax.axis_index(axis)
    block = own
    for step, mask in ring_masks(lax.axis_size(axis)):
        other = swap(block, axis, mask)
        upper = (pos & step) != 0
        block = jnp.where(upper, jnp.concatenate([other, block], axis=1), jnp.concatenate([block, other], axis=1))
    return block


def scatter_rows(value, axis):
    pos = lax.axis_index(axis)
    block = value
    for step, mask in reversed(ring_masks(lax.axis_size(axis))):
        half = block.shape[1] // 2
        upper = ((pos // step) % 2).astype(jnp.int32)
        keep = lax.dynamic_slice_in_dim(block, upper * half, half, 1)
        send = lax.dynamic_slice_in_dim(block, (1 - upper) * half, half, 1)
        block = keep + swap(send, axis, mask)
    return block


def all_sum(value, axes):
    for axis, rings in axes:
        masks = [0]
        scale = 1
        for ring in rings:
            masks += [mask * scale for _, mask in ring_masks(ring)]
            scale *= ring
        for mask in masks[1:]:
            value = value + swap(value, axis, mask)
    return value


def factor_kernel(gram_ref, upper_ref, inverse_ref):
    size = gram_ref.shape[0]
    mat = gram_ref[...]
    rows = lax.broadcasted_iota(jnp.int32, (size, size), 0)
    cols = lax.broadcasted_iota(jnp.int32, (size, size), 1)
    inv = (rows == cols).astype(jnp.float32)
    for j in range(size):
        col = jnp.sum(jnp.where(cols == j, mat, 0.0), axis=1, keepdims=True)
        row = jnp.sum(jnp.where(rows == j, mat, 0.0), axis=0, keepdims=True)
        inv_row = jnp.sum(jnp.where(rows == j, inv, 0.0), axis=0, keepdims=True)
        pivot = jnp.sum(jnp.where(rows[:, :1] == j, col, 0.0), axis=0, keepdims=True)
        scale = 1.0 / jnp.sqrt(pivot)
        ratio = jnp.where(rows[:, :1] > j, col / pivot, 0.0)
        here = rows == j
        mat = jnp.where(here, row * scale, mat - ratio * row)
        inv = jnp.where(here, inv_row * scale, inv - ratio * inv_row)
    upper_ref[...] = jnp.where(rows <= cols, mat, 0.0)
    inverse_ref[...] = jnp.where(rows >= cols, inv, 0.0)


def cholesky_parts(gram):
    size = gram.shape[0]
    shape = jax.ShapeDtypeStruct((size, size), jnp.float32)
    return pl.pallas_call(factor_kernel, out_shape=(shape, shape))((gram + gram.T) * 0.5)


def per_device(residual, factor, basis, send_rows):
    slab = residual.shape[2]
    row_count = lax.axis_size("row")
    sub_rows = slab * row_count
    total_rows = sub_rows * lax.axis_size("sub")
    own_rows = residual[:, 0, :]
    whole = gather_rows(own_rows, "row")
    index_rows = send_rows[0]
    to_lower = jnp.take(whole, index_rows[0], axis=1)
    to_upper = jnp.take(whole, index_rows[1], axis=1)
    from_lower = from_behind(to_upper, "sub", 1)
    from_upper = from_behind(to_lower, "sub", -1)
    factor_rows = factor[0]
    share = factor_rows.shape[0]
    margin = from_lower.shape[1]
    row_pos = lax.axis_index("row")
    three = lax.Precision.HIGH
    by_rows = (((1,), (1,)), ((), ()))
    start = row_pos * share
    inner_own = lax.optimization_barrier(lax.dot_general(whole, factor_rows[:, :sub_rows], by_rows, precision=three))
    margins = jnp.concatenate([from_lower, from_upper], axis=1)
    extended = jnp.concatenate([whole, margins], axis=1)
    inner = (
        inner_own
        + lax.dot_general(margins, factor_rows[:, sub_rows:], by_rows, precision=three)
        + lax.dynamic_slice_in_dim(extended, start, share, 1)
    )
    placed = lax.dynamic_update_slice_in_dim(jnp.zeros(extended.shape, jnp.float32), inner, start, 1)
    margin_value = jnp.dot(inner, factor_rows[:, sub_rows:], precision=three) + placed[:, sub_rows:]
    back_upper = from_behind(margin_value[:, :margin], "sub", -1)
    back_lower = from_behind(margin_value[:, margin:], "sub", 1)
    own_value = jnp.dot(inner, factor_rows[:, :sub_rows], precision=three) + placed[:, :sub_rows]
    all_rows = lax.iota(jnp.int32, sub_rows)
    select_upper = (index_rows[1][:, None] == all_rows[None, :]).astype(jnp.float32)
    select_lower = (index_rows[0][:, None] == all_rows[None, :]).astype(jnp.float32)
    gathered = (
        own_value
        + jnp.dot(back_upper, select_upper, precision=HIGH)
        + jnp.dot(back_lower, select_lower, precision=HIGH)
    )
    block_t = scatter_rows(gathered, "row")
    vectors = basis[:, 0, :]
    count = vectors.shape[0]
    vecs = block_t.shape[0]
    first_part = contract_rows(vectors, block_t)
    basis_gram = contract_rows(vectors, vectors)
    block_gram = contract_rows(block_t, block_t)
    packed = jnp.concatenate(
        [
            jnp.concatenate([first_part, basis_gram], axis=1),
            jnp.concatenate([block_gram, jnp.zeros((vecs, count), jnp.float32)], axis=1),
        ],
        axis=0,
    )
    summed = all_sum(packed, (("sub", (2, 4, lax.axis_size("sub") // 8)), ("row", (row_count,))))
    first, basis_gram, block_gram = lax.optimization_barrier(
        (summed[:count, :vecs], summed[:count, vecs:], summed[count:, :vecs])
    )
    second = first - jnp.dot(basis_gram, first, precision=HIGH)
    coeffs = first + second
    once = block_t - contract_first(first, vectors)
    twice = once - contract_first(second, vectors)
    cross = contract_first(first, coeffs)
    gram = (
        block_gram - cross - cross.T + contract_first(coeffs, jnp.dot(basis_gram, coeffs, precision=HIGH))
    ) / total_rows
    upper_tri, lower_inverse = cholesky_parts(gram)
    solved = jnp.dot(lower_inverse, twice, precision=HIGH)
    return (coeffs, upper_tri, solved[:, None, :])


def solution(mesh):
    placed = (
        P(None, "sub", "row"),
        P("sub", "row", None),
        P(None, "sub", "row"),
        P("sub", None, None),
    )
    return jax.shard_map(
        per_device,
        mesh=mesh,
        in_specs=placed,
        out_specs=(P(), P(), P(None, "sub", "row")),
        check_vma=False,
    )
```

```python
import jax
import jax.numpy as jnp
from jax import lax
from jax.experimental import pallas as pl
from jax.sharding import PartitionSpec as P

HIGH = lax.Precision.HIGHEST


def from_behind(value, axis, steps):
    count = lax.axis_size(axis)
    leading, last = (max(0, -steps), min(count, count - steps))
    return lax.ppermute(value, axis, [(source, source + steps) for source in range(leading, last)])


def swap(value, axis, mask):
    count = lax.axis_size(axis)
    return lax.ppermute(value, axis, [(source, source ^ mask) for source in range(count)])


def contract_rows(left_mat, right_mat):
    return lax.dot_general(left_mat, right_mat, (((1,), (1,)), ((), ())), precision=HIGH)


def contract_first(left_mat, right_mat):
    return lax.dot_general(left_mat, right_mat, (((0,), (0,)), ((), ())), precision=HIGH)


def ring_masks(size):
    near = {2: [1], 4: [1, 3], 8: [1, 2, 6]}
    masks = near.get(size) or [1 << b for b in range(size.bit_length() - 1)]
    return [(1 << b, mask) for b, mask in enumerate(masks)]


def gather_rows(own, axis):
    pos = lax.axis_index(axis)
    block = own
    for step, mask in ring_masks(lax.axis_size(axis)):
        other = swap(block, axis, mask)
        upper = (pos & step) != 0
        block = jnp.where(upper, jnp.concatenate([other, block], axis=1), jnp.concatenate([block, other], axis=1))
    return block


def scatter_rows(value, axis):
    pos = lax.axis_index(axis)
    block = value
    for step, mask in reversed(ring_masks(lax.axis_size(axis))):
        half = block.shape[1] // 2
        upper = ((pos // step) % 2).astype(jnp.int32)
        keep = lax.dynamic_slice_in_dim(block, upper * half, half, 1)
        send = lax.dynamic_slice_in_dim(block, (1 - upper) * half, half, 1)
        block = keep + swap(send, axis, mask)
    return block


def all_sum(value, axes):
    for axis, rings in axes:
        masks = [0]
        scale = 1
        for ring in rings:
            masks += [mask * scale for _, mask in ring_masks(ring)]
            scale *= ring
        for mask in masks[1:]:
            value = value + swap(value, axis, mask)
    return value


def factor_kernel(aug_ref, out_ref):
    size, width = aug_ref.shape
    aug = aug_ref[...]
    rows = lax.broadcasted_iota(jnp.int32, (size, width), 0)
    cols = lax.broadcasted_iota(jnp.int32, (size, width), 1)
    first_col = rows[:, :1]
    for j in range(size):
        col = jnp.sum(jnp.where(cols == j, aug, 0.0), axis=1, keepdims=True)
        row = jnp.sum(jnp.where(rows == j, aug, 0.0), axis=0, keepdims=True)
        pivot = jnp.sum(jnp.where(first_col == j, col, 0.0), axis=0, keepdims=True)
        ratio = jnp.where(first_col > j, col / pivot, 0.0)
        aug = jnp.where(rows == j, row * (1.0 / jnp.sqrt(pivot)), aug - ratio * row)
    out_ref[...] = jnp.where((rows <= cols) | (cols >= size), aug, 0.0)


def cholesky_parts(gram):
    size = gram.shape[0]
    aug = jnp.concatenate([(gram + gram.T) * 0.5, jnp.eye(size, dtype=jnp.float32)], axis=1)
    out = pl.pallas_call(factor_kernel, out_shape=jax.ShapeDtypeStruct(aug.shape, jnp.float32))(aug)
    return out[:, :size], out[:, size:]

def per_device(residual, factor, basis, send_rows):
    slab = residual.shape[2]
    row_count = lax.axis_size("row")
    sub_rows = slab * row_count
    total_rows = sub_rows * lax.axis_size("sub")
    own_rows = residual[:, 0, :]
    whole = gather_rows(own_rows, "row")
    index_rows = send_rows[0]
    both_sides = jnp.take(whole, index_rows.reshape(-1), axis=1)
    to_lower = both_sides[:, :index_rows.shape[1]]
    to_upper = both_sides[:, index_rows.shape[1]:]
    from_lower = from_behind(to_upper, "sub", 1)
    from_upper = from_behind(to_lower, "sub", -1)
    factor_rows = factor[0]
    share = factor_rows.shape[0]
    margin = from_lower.shape[1]
    row_pos = lax.axis_index("row")
    three = lax.Precision.HIGH
    by_rows = (((1,), (1,)), ((), ()))
    start = row_pos * share
    inner_own = lax.optimization_barrier(lax.dot_general(whole, factor_rows[:, :sub_rows], by_rows, precision=three))
    margins = jnp.concatenate([from_lower, from_upper], axis=1)
    extended = jnp.concatenate([whole, margins], axis=1)
    inner = (
        inner_own
        + lax.dot_general(margins, factor_rows[:, sub_rows:], by_rows, precision=three)
        + lax.dynamic_slice_in_dim(extended, start, share, 1)
    )
    placed = lax.dynamic_update_slice_in_dim(jnp.zeros(extended.shape, jnp.float32), inner, start, 1)
    margin_value = jnp.dot(inner, factor_rows[:, sub_rows:], precision=three) + placed[:, sub_rows:]
    back_upper = from_behind(margin_value[:, :margin], "sub", -1)
    back_lower = from_behind(margin_value[:, margin:], "sub", 1)
    own_value = jnp.dot(inner, factor_rows[:, :sub_rows], precision=three) + placed[:, :sub_rows]
    all_rows = lax.iota(jnp.int32, sub_rows)
    select_upper = (index_rows[1][:, None] == all_rows[None, :]).astype(jnp.float32)
    select_lower = (index_rows[0][:, None] == all_rows[None, :]).astype(jnp.float32)
    gathered = (
        own_value
        + jnp.dot(back_upper, select_upper, precision=HIGH)
        + jnp.dot(back_lower, select_lower, precision=HIGH)
    )
    block_t = scatter_rows(gathered, "row")
    vectors = basis[:, 0, :]
    count = vectors.shape[0]
    vecs = block_t.shape[0]
    first_part = contract_rows(vectors, block_t)
    basis_gram = contract_rows(vectors, vectors)
    block_gram = contract_rows(block_t, block_t)
    packed = jnp.concatenate(
        [
            jnp.concatenate([first_part, basis_gram], axis=1),
            jnp.concatenate([block_gram, jnp.zeros((vecs, count), jnp.float32)], axis=1),
        ],
        axis=0,
    )
    summed = all_sum(packed, (("sub", (2, 4, lax.axis_size("sub") // 8)), ("row", (row_count,))))
    first, basis_gram, block_gram = lax.optimization_barrier(
        (summed[:count, :vecs], summed[:count, vecs:], summed[count:, :vecs])
    )
    second = first - jnp.dot(basis_gram, first, precision=HIGH)
    coeffs = first + second
    once = block_t - contract_first(first, vectors)
    twice = once - contract_first(second, vectors)
    cross = contract_first(first, coeffs)
    gram = (
        block_gram - cross - cross.T + contract_first(coeffs, jnp.dot(basis_gram, coeffs, precision=HIGH))
    ) / total_rows
    upper_tri, lower_inverse = cholesky_parts(gram)
    solved = jnp.dot(lower_inverse, twice, precision=HIGH)
    return (coeffs, upper_tri, solved[:, None, :])


def solution(mesh):
    placed = (
        P(None, "sub", "row"),
        P("sub", "row", None),
        P(None, "sub", "row"),
        P("sub", None, None),
    )
    return jax.shard_map(
        per_device,
        mesh=mesh,
        in_specs=placed,
        out_specs=(P(), P(), P(None, "sub", "row")),
        check_vma=False,
    )
```

```python
import jax
import jax.numpy as jnp
from jax import lax
from jax.experimental import pallas as pl
from jax.sharding import PartitionSpec as P

HIGH = lax.Precision.HIGHEST


def from_behind(value, axis, steps):
    count = lax.axis_size(axis)
    leading, last = (max(0, -steps), min(count, count - steps))
    return lax.ppermute(value, axis, [(source, source + steps) for source in range(leading, last)])


def swap(value, axis, mask):
    count = lax.axis_size(axis)
    return lax.ppermute(value, axis, [(source, source ^ mask) for source in range(count)])


def contract_rows(left_mat, right_mat):
    return lax.dot_general(left_mat, right_mat, (((1,), (1,)), ((), ())), precision=HIGH)


def contract_first(left_mat, right_mat):
    return lax.dot_general(left_mat, right_mat, (((0,), (0,)), ((), ())), precision=HIGH)


def ring_masks(size):
    near = {2: [1], 4: [1, 3], 8: [1, 2, 6]}
    masks = near.get(size) or [1 << b for b in range(size.bit_length() - 1)]
    return [(1 << b, mask) for b, mask in enumerate(masks)]


def gather_rows(own, axis):
    pos = lax.axis_index(axis)
    block = own
    for step, mask in ring_masks(lax.axis_size(axis)):
        other = swap(block, axis, mask)
        upper = (pos & step) != 0
        block = jnp.where(upper, jnp.concatenate([other, block], axis=1), jnp.concatenate([block, other], axis=1))
    return block


def scatter_rows(value, axis):
    pos = lax.axis_index(axis)
    block = value
    for step, mask in reversed(ring_masks(lax.axis_size(axis))):
        half = block.shape[1] // 2
        upper = ((pos // step) % 2).astype(jnp.int32)
        keep = lax.dynamic_slice_in_dim(block, upper * half, half, 1)
        send = lax.dynamic_slice_in_dim(block, (1 - upper) * half, half, 1)
        block = keep + swap(send, axis, mask)
    return block


def all_sum(value, axes):
    for axis, rings in axes:
        masks = [0]
        scale = 1
        for ring in rings:
            masks += [mask * scale for _, mask in ring_masks(ring)]
            scale *= ring
        for mask in masks[1:]:
            value = value + swap(value, axis, mask)
    return value


def factor_kernel(gram_ref, upper_ref, inverse_ref):
    size = gram_ref.shape[0]
    mat = gram_ref[...]
    rows = lax.broadcasted_iota(jnp.int32, (size, size), 0)
    cols = lax.broadcasted_iota(jnp.int32, (size, size), 1)
    inv = (rows == cols).astype(jnp.float32)
    for j in range(size):
        col = jnp.sum(jnp.where(cols == j, mat, 0.0), axis=1, keepdims=True)
        row = jnp.sum(jnp.where(rows == j, mat, 0.0), axis=0, keepdims=True)
        inv_row = jnp.sum(jnp.where(rows == j, inv, 0.0), axis=0, keepdims=True)
        pivot = jnp.sum(jnp.where(rows[:, :1] == j, col, 0.0), axis=0, keepdims=True)
        scale = 1.0 / jnp.sqrt(pivot)
        ratio = jnp.where(rows[:, :1] > j, col / pivot, 0.0)
        here = rows == j
        mat = jnp.where(here, row * scale, mat - ratio * row)
        inv = jnp.where(here, inv_row * scale, inv - ratio * inv_row)
    upper_ref[...] = jnp.where(rows <= cols, mat, 0.0)
    inverse_ref[...] = jnp.where(rows >= cols, inv, 0.0)


def cholesky_parts(gram):
    size = gram.shape[0]
    shape = jax.ShapeDtypeStruct((size, size), jnp.float32)
    return pl.pallas_call(factor_kernel, out_shape=(shape, shape))((gram + gram.T) * 0.5)


def per_device(residual, factor, basis, send_rows):
    slab = residual.shape[2]
    row_count = lax.axis_size("row")
    sub_rows = slab * row_count
    total_rows = sub_rows * lax.axis_size("sub")
    own_rows = residual[:, 0, :]
    whole = gather_rows(own_rows, "row")
    index_rows = send_rows[0]
    to_lower = jnp.take(whole, index_rows[0], axis=1)
    to_upper = jnp.take(whole, index_rows[1], axis=1)
    from_lower = from_behind(to_upper, "sub", 1)
    from_upper = from_behind(to_lower, "sub", -1)
    factor_rows = factor[0]
    share = factor_rows.shape[0]
    margin = from_lower.shape[1]
    row_pos = lax.axis_index("row")
    three = lax.Precision.HIGH
    by_rows = (((1,), (1,)), ((), ()))
    start = row_pos * share
    inner_own = lax.optimization_barrier(lax.dot_general(whole, factor_rows[:, :sub_rows], by_rows, precision=three))
    margins = jnp.concatenate([from_lower, from_upper], axis=1)
    extended = jnp.concatenate([whole, margins], axis=1)
    inner = (
        inner_own
        + lax.dot_general(margins, factor_rows[:, sub_rows:], by_rows, precision=three)
        + lax.dynamic_slice_in_dim(extended, start, share, 1)
    )
    placed = lax.dynamic_update_slice_in_dim(jnp.zeros(extended.shape, jnp.float32), inner, start, 1)
    margin_value = jnp.dot(inner, factor_rows[:, sub_rows:], precision=three) + placed[:, sub_rows:]
    back_upper = from_behind(margin_value[:, :margin], "sub", -1)
    back_lower = from_behind(margin_value[:, margin:], "sub", 1)
    own_value = jnp.dot(inner, factor_rows[:, :sub_rows], precision=three) + placed[:, :sub_rows]
    all_rows = lax.iota(jnp.int32, sub_rows)
    select_upper = (index_rows[1][:, None] == all_rows[None, :]).astype(jnp.float32)
    select_lower = (index_rows[0][:, None] == all_rows[None, :]).astype(jnp.float32)
    gathered = (
        own_value
        + jnp.dot(back_upper, select_upper, precision=three)
        + jnp.dot(back_lower, select_lower, precision=three)
    )
    block_t = scatter_rows(gathered, "row")
    vectors = basis[:, 0, :]
    count = vectors.shape[0]
    vecs = block_t.shape[0]
    first_part = contract_rows(vectors, block_t)
    basis_gram = contract_rows(vectors, vectors)
    block_gram = contract_rows(block_t, block_t)
    packed = jnp.concatenate(
        [
            jnp.concatenate([first_part, basis_gram], axis=1),
            jnp.concatenate([block_gram, jnp.zeros((vecs, count), jnp.float32)], axis=1),
        ],
        axis=0,
    )
    summed = all_sum(packed, (("sub", (2, 4, lax.axis_size("sub") // 8)), ("row", (row_count,))))
    first, basis_gram, block_gram = lax.optimization_barrier(
        (summed[:count, :vecs], summed[:count, vecs:], summed[count:, :vecs])
    )
    second = first - jnp.dot(basis_gram, first, precision=HIGH)
    coeffs = first + second
    once = block_t - contract_first(first, vectors)
    twice = once - contract_first(second, vectors)
    cross = contract_first(first, coeffs)
    gram = (
        block_gram - cross - cross.T + contract_first(coeffs, jnp.dot(basis_gram, coeffs, precision=HIGH))
    ) / total_rows
    upper_tri, lower_inverse = cholesky_parts(gram)
    solved = jnp.dot(lower_inverse, twice, precision=HIGH)
    return (coeffs, upper_tri, solved[:, None, :])


def solution(mesh):
    placed = (
        P(None, "sub", "row"),
        P("sub", "row", None),
        P(None, "sub", "row"),
        P("sub", None, None),
    )
    return jax.shard_map(
        per_device,
        mesh=mesh,
        in_specs=placed,
        out_specs=(P(), P(), P(None, "sub", "row")),
        check_vma=False,
    )
```

```python
import jax
import jax.numpy as jnp
from jax import lax
from jax.experimental import pallas as pl
from jax.sharding import PartitionSpec as P

HIGH = lax.Precision.HIGHEST


def from_behind(value, axis, steps):
    count = lax.axis_size(axis)
    leading, last = (max(0, -steps), min(count, count - steps))
    return lax.ppermute(value, axis, [(source, source + steps) for source in range(leading, last)])


def swap(value, axis, mask):
    count = lax.axis_size(axis)
    return lax.ppermute(value, axis, [(source, source ^ mask) for source in range(count)])


def contract_rows(left_mat, right_mat):
    return lax.dot_general(left_mat, right_mat, (((1,), (1,)), ((), ())), precision=HIGH)


def contract_first(left_mat, right_mat):
    return lax.dot_general(left_mat, right_mat, (((0,), (0,)), ((), ())), precision=HIGH)


def ring_masks(size):
    near = {2: [1], 4: [1, 3], 8: [1, 2, 6]}
    masks = near.get(size) or [1 << b for b in range(size.bit_length() - 1)]
    return [(1 << b, mask) for b, mask in enumerate(masks)]


def gather_rows(own, axis):
    pos = lax.axis_index(axis)
    block = own
    for step, mask in ring_masks(lax.axis_size(axis)):
        other = swap(block, axis, mask)
        upper = (pos & step) != 0
        block = jnp.where(upper, jnp.concatenate([other, block], axis=1), jnp.concatenate([block, other], axis=1))
    return block


def scatter_rows(value, axis):
    pos = lax.axis_index(axis)
    block = value
    for step, mask in reversed(ring_masks(lax.axis_size(axis))):
        half = block.shape[1] // 2
        upper = ((pos // step) % 2).astype(jnp.int32)
        keep = lax.dynamic_slice_in_dim(block, upper * half, half, 1)
        send = lax.dynamic_slice_in_dim(block, (1 - upper) * half, half, 1)
        block = keep + swap(send, axis, mask)
    return block


def all_sum(value, axes):
    for axis, rings in axes:
        masks = [0]
        scale = 1
        for ring in rings:
            masks += [mask * scale for _, mask in ring_masks(ring)]
            scale *= ring
        for mask in masks[1:]:
            value = value + swap(value, axis, mask)
    return value


def factor_kernel(gram_ref, upper_ref, inverse_ref):
    size = gram_ref.shape[0]
    mat = gram_ref[...]
    rows = lax.broadcasted_iota(jnp.int32, (size, size), 0)
    cols = lax.broadcasted_iota(jnp.int32, (size, size), 1)
    inv = (rows == cols).astype(jnp.float32)
    for j in range(size):
        col = jnp.sum(jnp.where(cols == j, mat, 0.0), axis=1, keepdims=True)
        row = jnp.sum(jnp.where(rows == j, mat, 0.0), axis=0, keepdims=True)
        inv_row = jnp.sum(jnp.where(rows == j, inv, 0.0), axis=0, keepdims=True)
        pivot = jnp.sum(jnp.where(rows[:, :1] == j, col, 0.0), axis=0, keepdims=True)
        scale = 1.0 / jnp.sqrt(pivot)
        ratio = jnp.where(rows[:, :1] > j, col / pivot, 0.0)
        here = rows == j
        mat = jnp.where(here, row * scale, mat - ratio * row)
        inv = jnp.where(here, inv_row * scale, inv - ratio * inv_row)
    upper_ref[...] = jnp.where(rows <= cols, mat, 0.0)
    inverse_ref[...] = jnp.where(rows >= cols, inv, 0.0)


def cholesky_parts(gram):
    size = gram.shape[0]
    shape = jax.ShapeDtypeStruct((size, size), jnp.float32)
    return pl.pallas_call(factor_kernel, out_shape=(shape, shape))((gram + gram.T) * 0.5)


def per_device(residual, factor, basis, send_rows):
    slab = residual.shape[2]
    row_count = lax.axis_size("row")
    sub_rows = slab * row_count
    total_rows = sub_rows * lax.axis_size("sub")
    own_rows = residual[:, 0, :]
    whole = gather_rows(own_rows, "row")
    index_rows = send_rows[0]
    to_lower = jnp.take(whole, index_rows[0], axis=1)
    to_upper = jnp.take(whole, index_rows[1], axis=1)
    from_lower = from_behind(to_upper, "sub", 1)
    from_upper = from_behind(to_lower, "sub", -1)
    factor_rows = factor[0]
    share = factor_rows.shape[0]
    margin = from_lower.shape[1]
    row_pos = lax.axis_index("row")
    three = lax.Precision.HIGH
    by_rows = (((1,), (1,)), ((), ()))
    start = row_pos * share
    inner_own = lax.optimization_barrier(lax.dot_general(whole, factor_rows[:, :sub_rows], by_rows, precision=three))
    margins = jnp.concatenate([from_lower, from_upper], axis=1)
    extended = jnp.concatenate([whole, margins], axis=1)
    inner = (
        inner_own
        + lax.dot_general(margins, factor_rows[:, sub_rows:], by_rows, precision=three)
        + lax.dynamic_slice_in_dim(extended, start, share, 1)
    )
    placed = lax.dynamic_update_slice_in_dim(jnp.zeros(extended.shape, jnp.float32), inner, start, 1)
    margin_value = jnp.dot(inner, factor_rows[:, sub_rows:], precision=three) + placed[:, sub_rows:]
    back_upper = from_behind(margin_value[:, :margin], "sub", -1)
    back_lower = from_behind(margin_value[:, margin:], "sub", 1)
    own_value = jnp.dot(inner, factor_rows[:, :sub_rows], precision=three) + placed[:, :sub_rows]
    all_rows = lax.iota(jnp.int32, sub_rows)
    select_upper = (index_rows[1][:, None] == all_rows[None, :]).astype(jnp.float32)
    select_lower = (index_rows[0][:, None] == all_rows[None, :]).astype(jnp.float32)
    gathered = (
        own_value
        + jnp.dot(back_upper, select_upper, precision=HIGH)
        + jnp.dot(back_lower, select_lower, precision=HIGH)
    )
    block_t = scatter_rows(gathered, "row")
    vectors = basis[:, 0, :]
    count = vectors.shape[0]
    vecs = block_t.shape[0]
    first_part = contract_rows(vectors, block_t)
    basis_gram = contract_rows(vectors, vectors)
    block_gram = contract_rows(block_t, block_t)
    packed = jnp.concatenate(
        [
            jnp.concatenate([first_part, basis_gram], axis=1),
            jnp.concatenate([block_gram, jnp.zeros((vecs, count), jnp.float32)], axis=1),
        ],
        axis=0,
    )
    summed = all_sum(packed, (("row", (row_count,)), ("sub", (2, 4, lax.axis_size("sub") // 8))))
    first, basis_gram, block_gram = lax.optimization_barrier(
        (summed[:count, :vecs], summed[:count, vecs:], summed[count:, :vecs])
    )
    second = first - jnp.dot(basis_gram, first, precision=HIGH)
    coeffs = first + second
    once = block_t - contract_first(first, vectors)
    twice = once - contract_first(second, vectors)
    cross = contract_first(first, coeffs)
    gram = (
        block_gram - cross - cross.T + contract_first(coeffs, jnp.dot(basis_gram, coeffs, precision=HIGH))
    ) / total_rows
    upper_tri, lower_inverse = cholesky_parts(gram)
    solved = jnp.dot(lower_inverse, twice, precision=HIGH)
    return (coeffs, upper_tri, solved[:, None, :])


def solution(mesh):
    placed = (
        P(None, "sub", "row"),
        P("sub", "row", None),
        P(None, "sub", "row"),
        P("sub", None, None),
    )
    return jax.shard_map(
        per_device,
        mesh=mesh,
        in_specs=placed,
        out_specs=(P(), P(), P(None, "sub", "row")),
        check_vma=False,
    )
```

```python
import jax
import jax.numpy as jnp
from jax import lax
from jax.experimental import pallas as pl
from jax.sharding import PartitionSpec as P

HIGH = lax.Precision.HIGHEST


def from_behind(value, axis, steps):
    count = lax.axis_size(axis)
    leading, last = (max(0, -steps), min(count, count - steps))
    return lax.ppermute(value, axis, [(source, source + steps) for source in range(leading, last)])


def swap(value, axis, mask):
    count = lax.axis_size(axis)
    return lax.ppermute(value, axis, [(source, source ^ mask) for source in range(count)])


def contract_rows(left_mat, right_mat):
    return lax.dot_general(left_mat, right_mat, (((1,), (1,)), ((), ())), precision=HIGH)


def contract_first(left_mat, right_mat):
    return lax.dot_general(left_mat, right_mat, (((0,), (0,)), ((), ())), precision=HIGH)


def ring_masks(size):
    near = {2: [1], 4: [1, 3], 8: [1, 2, 6]}
    masks = near.get(size) or [1 << b for b in range(size.bit_length() - 1)]
    return [(1 << b, mask) for b, mask in enumerate(masks)]


def gather_rows(own, axis):
    pos = lax.axis_index(axis)
    block = own
    for step, mask in ring_masks(lax.axis_size(axis)):
        other = swap(block, axis, mask)
        upper = (pos & step) != 0
        block = jnp.where(upper, jnp.concatenate([other, block], axis=1), jnp.concatenate([block, other], axis=1))
    return block


def scatter_rows(value, axis):
    pos = lax.axis_index(axis)
    block = value
    for step, mask in reversed(ring_masks(lax.axis_size(axis))):
        half = block.shape[1] // 2
        upper = ((pos // step) % 2).astype(jnp.int32)
        keep = lax.dynamic_slice_in_dim(block, upper * half, half, 1)
        send = lax.dynamic_slice_in_dim(block, (1 - upper) * half, half, 1)
        block = keep + swap(send, axis, mask)
    return block


def all_sum(value, axes):
    for axis, rings in axes:
        masks = [0]
        scale = 1
        for ring in rings:
            masks += [mask * scale for _, mask in ring_masks(ring)]
            scale *= ring
        for mask in masks[1:]:
            value = value + swap(value, axis, mask)
    return value


def factor_kernel(gram_ref, upper_ref, inverse_ref):
    size = gram_ref.shape[0]
    mat = gram_ref[...]
    mat = (mat + mat.T) * 0.5
    rows = lax.broadcasted_iota(jnp.int32, (size, size), 0)
    cols = lax.broadcasted_iota(jnp.int32, (size, size), 1)
    inv = (rows == cols).astype(jnp.float32)
    for j in range(size):
        col = jnp.sum(jnp.where(cols == j, mat, 0.0), axis=1, keepdims=True)
        row = jnp.sum(jnp.where(rows == j, mat, 0.0), axis=0, keepdims=True)
        inv_row = jnp.sum(jnp.where(rows == j, inv, 0.0), axis=0, keepdims=True)
        pivot = jnp.sum(jnp.where(rows[:, :1] == j, col, 0.0), axis=0, keepdims=True)
        scale = 1.0 / jnp.sqrt(pivot)
        lower_col = jnp.where(rows[:, :1] > j, col * scale, 0.0)
        row = row * scale
        inv_row = inv_row * scale
        here = rows == j
        mat = jnp.where(here, row, mat - lower_col * row)
        inv = jnp.where(here, inv_row, inv - lower_col * inv_row)
    upper_ref[...] = jnp.where(rows <= cols, mat, 0.0)
    inverse_ref[...] = jnp.where(rows >= cols, inv, 0.0)


def cholesky_parts(gram):
    size = gram.shape[0]
    shape = jax.ShapeDtypeStruct((size, size), jnp.float32)
    return pl.pallas_call(factor_kernel, out_shape=(shape, shape))(gram)

def per_device(residual, factor, basis, send_rows):
    slab = residual.shape[2]
    row_count = lax.axis_size("row")
    sub_rows = slab * row_count
    total_rows = sub_rows * lax.axis_size("sub")
    own_rows = residual[:, 0, :]
    whole = gather_rows(own_rows, "row")
    index_rows = send_rows[0]
    to_lower = jnp.take(whole, index_rows[0], axis=1)
    to_upper = jnp.take(whole, index_rows[1], axis=1)
    from_lower = from_behind(to_upper, "sub", 1)
    from_upper = from_behind(to_lower, "sub", -1)
    factor_rows = factor[0]
    share = factor_rows.shape[0]
    margin = from_lower.shape[1]
    row_pos = lax.axis_index("row")
    three = lax.Precision.HIGH
    by_rows = (((1,), (1,)), ((), ()))
    start = row_pos * share
    inner_own = lax.optimization_barrier(lax.dot_general(whole, factor_rows[:, :sub_rows], by_rows, precision=three))
    margins = jnp.concatenate([from_lower, from_upper], axis=1)
    extended = jnp.concatenate([whole, margins], axis=1)
    inner = (
        inner_own
        + lax.dot_general(margins, factor_rows[:, sub_rows:], by_rows, precision=three)
        + lax.dynamic_slice_in_dim(extended, start, share, 1)
    )
    placed = lax.dynamic_update_slice_in_dim(jnp.zeros(extended.shape, jnp.float32), inner, start, 1)
    margin_value = jnp.dot(inner, factor_rows[:, sub_rows:], precision=three) + placed[:, sub_rows:]
    back_upper = from_behind(margin_value[:, :margin], "sub", -1)
    back_lower = from_behind(margin_value[:, margin:], "sub", 1)
    own_value = jnp.dot(inner, factor_rows[:, :sub_rows], precision=three) + placed[:, :sub_rows]
    all_rows = lax.iota(jnp.int32, sub_rows)
    select_upper = (index_rows[1][:, None] == all_rows[None, :]).astype(jnp.float32)
    select_lower = (index_rows[0][:, None] == all_rows[None, :]).astype(jnp.float32)
    gathered = (
        own_value
        + jnp.dot(back_upper, select_upper, precision=HIGH)
        + jnp.dot(back_lower, select_lower, precision=HIGH)
    )
    block_t = scatter_rows(gathered, "row")
    vectors = basis[:, 0, :]
    count = vectors.shape[0]
    vecs = block_t.shape[0]
    first_part = contract_rows(vectors, block_t)
    basis_gram = contract_rows(vectors, vectors)
    block_gram = contract_rows(block_t, block_t)
    packed = jnp.concatenate(
        [
            jnp.concatenate([first_part, basis_gram], axis=1),
            jnp.concatenate([block_gram, jnp.zeros((vecs, count), jnp.float32)], axis=1),
        ],
        axis=0,
    )
    summed = all_sum(packed, (("sub", (2, 4, lax.axis_size("sub") // 8)), ("row", (row_count,))))
    first, basis_gram, block_gram = lax.optimization_barrier(
        (summed[:count, :vecs], summed[:count, vecs:], summed[count:, :vecs])
    )
    second = first - jnp.dot(basis_gram, first, precision=HIGH)
    coeffs = first + second
    once = block_t - contract_first(first, vectors)
    twice = once - contract_first(second, vectors)
    cross = contract_first(first, coeffs)
    gram = (
        block_gram - cross - cross.T + contract_first(coeffs, jnp.dot(basis_gram, coeffs, precision=HIGH))
    ) / total_rows
    upper_tri, lower_inverse = cholesky_parts(gram)
    solved = jnp.dot(lower_inverse, twice, precision=HIGH)
    return (coeffs, upper_tri, solved[:, None, :])


def solution(mesh):
    placed = (
        P(None, "sub", "row"),
        P("sub", "row", None),
        P(None, "sub", "row"),
        P("sub", None, None),
    )
    return jax.shard_map(
        per_device,
        mesh=mesh,
        in_specs=placed,
        out_specs=(P(), P(), P(None, "sub", "row")),
        check_vma=False,
    )
```

```python
import jax
import jax.numpy as jnp
from jax import lax
from jax.experimental import pallas as pl
from jax.sharding import PartitionSpec as P

HIGH = lax.Precision.HIGHEST


def from_behind(value, axis, steps):
    count = lax.axis_size(axis)
    leading, last = (max(0, -steps), min(count, count - steps))
    return lax.ppermute(value, axis, [(source, source + steps) for source in range(leading, last)])


def swap(value, axis, mask):
    count = lax.axis_size(axis)
    return lax.ppermute(value, axis, [(source, source ^ mask) for source in range(count)])


def contract_rows(left_mat, right_mat):
    return lax.dot_general(left_mat, right_mat, (((1,), (1,)), ((), ())), precision=HIGH)


def contract_first(left_mat, right_mat):
    return lax.dot_general(left_mat, right_mat, (((0,), (0,)), ((), ())), precision=HIGH)


def ring_masks(size):
    near = {2: [1], 4: [1, 3], 8: [1, 2, 6]}
    masks = near.get(size) or [1 << b for b in range(size.bit_length() - 1)]
    return [(1 << b, mask) for b, mask in enumerate(masks)]


def gather_rows(own, axis):
    pos = lax.axis_index(axis)
    block = own
    for step, mask in ring_masks(lax.axis_size(axis)):
        other = swap(block, axis, mask)
        upper = (pos & step) != 0
        block = jnp.where(upper, jnp.concatenate([other, block], axis=1), jnp.concatenate([block, other], axis=1))
    return block


def scatter_rows(value, axis):
    pos = lax.axis_index(axis)
    block = value
    for step, mask in reversed(ring_masks(lax.axis_size(axis))):
        half = block.shape[1] // 2
        upper = ((pos // step) % 2).astype(jnp.int32)
        keep = lax.dynamic_slice_in_dim(block, upper * half, half, 1)
        send = lax.dynamic_slice_in_dim(block, (1 - upper) * half, half, 1)
        block = keep + swap(send, axis, mask)
    return block


def all_sum(value, axes):
    for axis, rings in axes:
        masks = [0]
        scale = 1
        for ring in rings:
            masks += [mask * scale for _, mask in ring_masks(ring)]
            scale *= ring
        for mask in masks[1:]:
            value = value + swap(value, axis, mask)
    return value


def factor_kernel(gram_ref, upper_ref, inverse_ref):
    size = gram_ref.shape[0]
    mat = gram_ref[...]
    rows = lax.broadcasted_iota(jnp.int32, (size, size), 0)
    cols = lax.broadcasted_iota(jnp.int32, (size, size), 1)
    inv = (rows == cols).astype(jnp.float32)
    for j in range(size):
        col = jnp.sum(jnp.where(cols == j, mat, 0.0), axis=1, keepdims=True)
        row = jnp.sum(jnp.where(rows == j, mat, 0.0), axis=0, keepdims=True)
        inv_row = jnp.sum(jnp.where(rows == j, inv, 0.0), axis=0, keepdims=True)
        pivot = jnp.sum(jnp.where(rows[:, :1] == j, col, 0.0), axis=0, keepdims=True)
        scale = 1.0 / jnp.sqrt(pivot)
        ratio = jnp.where(rows[:, :1] > j, col / pivot, 0.0)
        here = rows == j
        mat = jnp.where(here, row * scale, mat - ratio * row)
        inv = jnp.where(here, inv_row * scale, inv - ratio * inv_row)
    upper_ref[...] = jnp.where(rows <= cols, mat, 0.0)
    inverse_ref[...] = jnp.where(rows >= cols, inv, 0.0)


def cholesky_parts(gram):
    size = gram.shape[0]
    shape = jax.ShapeDtypeStruct((size, size), jnp.float32)
    return pl.pallas_call(factor_kernel, out_shape=(shape, shape))((gram + gram.T) * 0.5)


def per_device(residual, factor, basis, send_rows):
    slab = residual.shape[2]
    row_count = lax.axis_size("row")
    sub_rows = slab * row_count
    total_rows = sub_rows * lax.axis_size("sub")
    own_rows = residual[:, 0, :]
    whole = gather_rows(own_rows, "row")
    index_rows = send_rows[0]
    to_lower = jnp.take(whole, index_rows[0], axis=1)
    to_upper = jnp.take(whole, index_rows[1], axis=1)
    from_lower = from_behind(to_upper, "sub", 1)
    from_upper = from_behind(to_lower, "sub", -1)
    factor_rows = factor[0]
    share = factor_rows.shape[0]
    margin = from_lower.shape[1]
    row_pos = lax.axis_index("row")
    three = lax.Precision.HIGH
    by_rows = (((1,), (1,)), ((), ()))
    start = row_pos * share
    extended = jnp.concatenate([whole, from_lower, from_upper], axis=1)
    inner = lax.dynamic_slice_in_dim(extended, start, share, 1) + lax.dot_general(
        extended, factor_rows, by_rows, precision=three
    )
    placed = lax.dynamic_update_slice_in_dim(jnp.zeros(extended.shape, jnp.float32), inner, start, 1)
    margin_value = jnp.dot(inner, factor_rows[:, sub_rows:], precision=three) + placed[:, sub_rows:]
    back_upper = from_behind(margin_value[:, :margin], "sub", -1)
    back_lower = from_behind(margin_value[:, margin:], "sub", 1)
    own_value = jnp.dot(inner, factor_rows[:, :sub_rows], precision=three) + placed[:, :sub_rows]
    all_rows = lax.iota(jnp.int32, sub_rows)
    select_upper = (index_rows[1][:, None] == all_rows[None, :]).astype(jnp.float32)
    select_lower = (index_rows[0][:, None] == all_rows[None, :]).astype(jnp.float32)
    gathered = (
        own_value
        + jnp.dot(back_upper, select_upper, precision=HIGH)
        + jnp.dot(back_lower, select_lower, precision=HIGH)
    )
    block_t = scatter_rows(gathered, "row")
    vectors = basis[:, 0, :]
    count = vectors.shape[0]
    vecs = block_t.shape[0]
    first_part = contract_rows(vectors, block_t)
    basis_gram = contract_rows(vectors, vectors)
    block_gram = contract_rows(block_t, block_t)
    packed = jnp.concatenate(
        [
            jnp.concatenate([first_part, basis_gram], axis=1),
            jnp.concatenate([block_gram, jnp.zeros((vecs, count), jnp.float32)], axis=1),
        ],
        axis=0,
    )
    summed = all_sum(packed, (("sub", (2, 4, lax.axis_size("sub") // 8)), ("row", (row_count,))))
    first, basis_gram, block_gram = lax.optimization_barrier(
        (summed[:count, :vecs], summed[:count, vecs:], summed[count:, :vecs])
    )
    second = first - jnp.dot(basis_gram, first, precision=HIGH)
    coeffs = first + second
    once = block_t - contract_first(first, vectors)
    twice = once - contract_first(second, vectors)
    cross = contract_first(first, coeffs)
    gram = (
        block_gram - cross - cross.T + contract_first(coeffs, jnp.dot(basis_gram, coeffs, precision=HIGH))
    ) / total_rows
    upper_tri, lower_inverse = cholesky_parts(gram)
    solved = jnp.dot(lower_inverse, twice, precision=HIGH)
    return (coeffs, upper_tri, solved[:, None, :])


def solution(mesh):
    placed = (
        P(None, "sub", "row"),
        P("sub", "row", None),
        P(None, "sub", "row"),
        P("sub", None, None),
    )
    return jax.shard_map(
        per_device,
        mesh=mesh,
        in_specs=placed,
        out_specs=(P(), P(), P(None, "sub", "row")),
        check_vma=False,
    )
```

```python
import jax
import jax.numpy as jnp
from jax import lax
from jax.experimental import pallas as pl
from jax.sharding import PartitionSpec as P


HIGH = lax.Precision.HIGHEST


def from_behind(value, axis, steps):
    count = lax.axis_size(axis)
    leading, last = (max(0, -steps), min(count, count - steps))
    return lax.ppermute(value, axis, [(source, source + steps) for source in range(leading, last)])


def swap(value, axis, mask):
    count = lax.axis_size(axis)
    return lax.ppermute(value, axis, [(source, source ^ mask) for source in range(count)])


def contract_rows(left_mat, right_mat):
    return lax.dot_general(left_mat, right_mat, (((1,), (1,)), ((), ())), precision=HIGH)


def contract_first(left_mat, right_mat):
    return lax.dot_general(left_mat, right_mat, (((0,), (0,)), ((), ())), precision=HIGH)


def ring_masks(size):
    near = {2: [1], 4: [1, 3], 8: [1, 2, 6]}
    masks = near.get(size) or [1 << b for b in range(size.bit_length() - 1)]
    return [(1 << b, mask) for b, mask in enumerate(masks)]


def gather_rows(own, axis):
    pos = lax.axis_index(axis)
    block = own
    for step, mask in ring_masks(lax.axis_size(axis)):
        other = swap(block, axis, mask)
        upper = (pos & step) != 0
        block = jnp.where(upper, jnp.concatenate([other, block], axis=1), jnp.concatenate([block, other], axis=1))
    return block


def all_sum(value, axes):
    for axis, rings in axes:
        masks = [0]
        scale = 1
        for ring in rings:
            masks += [mask * scale for _, mask in ring_masks(ring)]
            scale *= ring
        for mask in masks[1:]:
            value = value + swap(value, axis, mask)
    return value


def factor_kernel(gram_ref, upper_ref, inverse_ref):
    size = gram_ref.shape[0]
    mat = gram_ref[...]
    rows = lax.broadcasted_iota(jnp.int32, (size, size), 0)
    cols = lax.broadcasted_iota(jnp.int32, (size, size), 1)
    inv = (rows == cols).astype(jnp.float32)
    for j in range(size):
        col = jnp.sum(jnp.where(cols == j, mat, 0.0), axis=1, keepdims=True)
        row = jnp.sum(jnp.where(rows == j, mat, 0.0), axis=0, keepdims=True)
        inv_row = jnp.sum(jnp.where(rows == j, inv, 0.0), axis=0, keepdims=True)
        pivot = jnp.sum(jnp.where(rows[:, :1] == j, col, 0.0), axis=0, keepdims=True)
        scale = 1.0 / jnp.sqrt(pivot)
        ratio = jnp.where(rows[:, :1] > j, col / pivot, 0.0)
        here = rows == j
        mat = jnp.where(here, row * scale, mat - ratio * row)
        inv = jnp.where(here, inv_row * scale, inv - ratio * inv_row)
    upper_ref[...] = jnp.where(rows <= cols, mat, 0.0)
    inverse_ref[...] = jnp.where(rows >= cols, inv, 0.0)


def cholesky_parts(gram):
    size = gram.shape[0]
    shape = jax.ShapeDtypeStruct((size, size), jnp.float32)
    return pl.pallas_call(factor_kernel, out_shape=(shape, shape))((gram + gram.T) * 0.5)


def per_device(residual, factor, basis, send_rows):
    slab = residual.shape[2]
    row_count = lax.axis_size("row")
    sub_rows = slab * row_count
    total_rows = sub_rows * lax.axis_size("sub")
    own_rows = residual[:, 0, :]
    whole = gather_rows(own_rows, "row")
    index_rows = send_rows[0]
    to_lower = jnp.take(whole, index_rows[0], axis=1)
    to_upper = jnp.take(whole, index_rows[1], axis=1)
    from_lower = from_behind(to_upper, "sub", 1)
    from_upper = from_behind(to_lower, "sub", -1)
    factor_rows = factor[0]
    share = factor_rows.shape[0]
    margin = from_lower.shape[1]
    row_pos = lax.axis_index("row")
    three = lax.Precision.HIGH
    by_rows = (((1,), (1,)), ((), ()))
    start = row_pos * share
    inner_own = lax.optimization_barrier(lax.dot_general(whole, factor_rows[:, :sub_rows], by_rows, precision=three))
    margins = jnp.concatenate([from_lower, from_upper], axis=1)
    extended = jnp.concatenate([whole, margins], axis=1)
    inner = (
        inner_own
        + lax.dot_general(margins, factor_rows[:, sub_rows:], by_rows, precision=three)
        + lax.dynamic_slice_in_dim(extended, start, share, 1)
    )
    placed = lax.dynamic_update_slice_in_dim(jnp.zeros(extended.shape, jnp.float32), inner, start, 1)
    margin_value = jnp.dot(inner, factor_rows[:, sub_rows:], precision=three) + placed[:, sub_rows:]
    back_upper = from_behind(margin_value[:, :margin], "sub", -1)
    back_lower = from_behind(margin_value[:, margin:], "sub", 1)
    own_value = jnp.dot(inner, factor_rows[:, :sub_rows], precision=three) + placed[:, :sub_rows]
    half = sub_rows // 2

    def half_value(which):
        rows_here = which * half + lax.iota(jnp.int32, half)
        select_upper = (index_rows[1][:, None] == rows_here[None, :]).astype(jnp.float32)
        select_lower = (index_rows[0][:, None] == rows_here[None, :]).astype(jnp.float32)
        return (
            lax.dynamic_slice_in_dim(own_value, which * half, half, 1)
            + jnp.dot(back_upper, select_upper, precision=HIGH)
            + jnp.dot(back_lower, select_lower, precision=HIGH)
        )

    (step, mask), rest = ring_masks(row_count)[-1], ring_masks(row_count)[:-1]
    keep_upper = ((row_pos // step) % 2).astype(jnp.int32)
    block_t = half_value(keep_upper) + swap(half_value(1 - keep_upper), "row", mask)
    for step, mask in reversed(rest):
        part = block_t.shape[1] // 2
        upper = ((row_pos // step) % 2).astype(jnp.int32)
        keep = lax.dynamic_slice_in_dim(block_t, upper * part, part, 1)
        send = lax.dynamic_slice_in_dim(block_t, (1 - upper) * part, part, 1)
        block_t = keep + swap(send, "row", mask)
    vectors = basis[:, 0, :]
    count = vectors.shape[0]
    vecs = block_t.shape[0]
    first_part = contract_rows(vectors, block_t)
    basis_gram = contract_rows(vectors, vectors)
    block_gram = contract_rows(block_t, block_t)
    packed = jnp.concatenate(
        [
            jnp.concatenate([first_part, basis_gram], axis=1),
            jnp.concatenate([block_gram, jnp.zeros((vecs, count), jnp.float32)], axis=1),
        ],
        axis=0,
    )
    summed = all_sum(packed, (("sub", (2, 4, lax.axis_size("sub") // 8)), ("row", (row_count,))))
    first, basis_gram, block_gram = lax.optimization_barrier(
        (summed[:count, :vecs], summed[:count, vecs:], summed[count:, :vecs])
    )
    second = first - jnp.dot(basis_gram, first, precision=HIGH)
    coeffs = first + second
    once = block_t - contract_first(first, vectors)
    twice = once - contract_first(second, vectors)
    cross = contract_first(first, coeffs)
    gram = (
        block_gram - cross - cross.T + contract_first(coeffs, jnp.dot(basis_gram, coeffs, precision=HIGH))
    ) / total_rows
    upper_tri, lower_inverse = cholesky_parts(gram)
    solved = jnp.dot(lower_inverse, twice, precision=HIGH)
    return (coeffs, upper_tri, solved[:, None, :])


def solution(mesh):
    placed = (
        P(None, "sub", "row"),
        P("sub", "row", None),
        P(None, "sub", "row"),
        P("sub", None, None),
    )

    return jax.shard_map(
        per_device,
        mesh=mesh,
        in_specs=placed,
        out_specs=(P(), P(), P(None, "sub", "row")),
        check_vma=False,
    )
```
